1024 devices in a mesh: tm: 8 (over x, core), rows: 128 (over z, y).
Axes of the slice: x: 4, y: 8, z: 16, core: 2. Of those that a mesh axis runs over, the one named last changes fastest.
Arguments:
- video: bfloat16 [16, 256, 128, 128], P('tm', 'rows'), may hold values from -6 to 6
- kernel: bfloat16 [3, 3, 3, 128, 128], replicated, may hold values from -0.109375 to 0.109375
- cotangent: bfloat16 [16, 256, 128, 128], P('tm', 'rows'), may hold values from -24 to 24
Outputs:
- activated: bfloat16 [16, 256, 128, 128], P('tm', 'rows')
- input_grad: bfloat16 [16, 256, 128, 128], P('tm', 'rows')
- kernel_grad: float32 [128, 3456], P('rows', 'tm')
The draws below stay inside these ranges and needn't reach their ends.
All inputs are finite; a program needn't handle non-finite values.
Results may differ from the reference program's by a relative error of at most 0.0049.
Values may be sent and summed in bfloat16 or wider, within the bound.
No kernel may reach another device: no remote copies, remote signals or barrier semaphores. Data moves between devices by JAX's collectives and lax.ppermute only.
A program may use at most 32 MiB of HBM per device.

```python
import jax
import jax.numpy as jnp
from jax import lax

C = 128
W = 128
FRAMES = 16
H = 256


def raised(drawn, stream_key, source, target, blocks, factor):
    def block_of(dim):
        return (jnp.arange(drawn.shape[dim]) // (drawn.shape[dim] // blocks)).reshape((-1,) + (1,) * (drawn.ndim - 1 - dim))

    near = jax.random.permutation(stream_key, blocks)[block_of(target)]
    other_side = (block_of(target) + blocks // 2) % blocks
    return jnp.where((block_of(source) == near) | (block_of(source) == other_side), factor * drawn, drawn)


def levels(stream_key, shape, shards, least, top_value):
    factor_of = 1.0
    for axis_at, parts in shards:
        heights = jax.random.uniform(jax.random.fold_in(jax.random.fold_in(stream_key, 6), axis_at), (parts,), jnp.float32, least / len(shards), top_value / len(shards))
        factor_of = factor_of * jnp.repeat(jnp.exp(heights), shape[axis_at] // parts).reshape((-1,) + (1,) * (len(shape) - 1 - axis_at))
    return factor_of


def noise(own_key, shape, scale, most, cuts=(), dtype=jnp.bfloat16):
    drawn = scale * jax.random.normal(own_key, shape, jnp.float32)
    if cuts:
        drawn = drawn * levels(own_key, shape, cuts, -0.22, 0.18)
    return jnp.clip(drawn, -most, most).astype(dtype)


def gaussian_with(stream_key, dims, scale, bound, split, heavy, kind=jnp.bfloat16):
    result = scale * jax.random.normal(stream_key, dims, jnp.float32)
    if split:
        result = result * levels(stream_key, dims, split, -0.22, 0.18)
    return jnp.clip(raised(result, jax.random.fold_in(stream_key, 3), *heavy), -bound, bound).astype(kind)


def setup_inputs(seed: int = 0) -> dict:
    key_list = jax.random.split(jax.random.key(seed), 4)
    return {
        "video": noise(key_list[0], (FRAMES, H, W, C), 1.0, 6.0, ((0, 8), (1, 128))),
        "kernel": noise(key_list[1], (3, 3, 3, C, C), (27 * C) ** -0.5, 0.109375),
        "cotangent": gaussian_with(key_list[2], (FRAMES, H, W, C), 1.0, 24.0, ((0, 8), (1, 128)), (1, 3, 128, 5.5)),
    }


def conv3(padded, kmat):
    lhs = padded.astype(jnp.float32)[None]
    rhs = kmat.astype(jnp.float32)
    out = lax.conv_general_dilated(lhs, rhs, (1, 1, 1), "VALID", dimension_numbers=("NDHWC", "DHWIO", "NDHWC"), precision=lax.Precision.HIGHEST)
    return out[0]


def reference(video, kernel, cotangent):
    padded = jnp.pad(video, ((2, 0), (1, 1), (1, 1), (0, 0)))
    pre = conv3(padded, kernel)
    sig = 1.0 / (1.0 + jnp.exp(-pre))
    activated = (pre * sig).astype(jnp.bfloat16)
    pre_grad = (cotangent.astype(jnp.float32) * sig * (1.0 + pre * (1.0 - sig))).astype(jnp.bfloat16)
    grad_padded = jnp.pad(pre_grad, ((0, 2), (1, 1), (1, 1), (0, 0)))
    flipped = jnp.transpose(kernel[::-1, ::-1, ::-1], (0, 1, 2, 4, 3))
    input_grad = conv3(grad_padded, flipped).astype(jnp.bfloat16)
    grad_float = pre_grad.astype(jnp.float32)
    padded_float = padded.astype(jnp.float32)
    blocks = []
    for a in range(3):
        for b in range(3):
            for c in range(3):
                window = padded_float[a:a + FRAMES, b:b + H, c:c + W]
                blocks.append(jnp.einsum("thwi,thwo->oi", window, grad_float, precision=lax.Precision.HIGHEST))
    kernel_grad = jnp.concatenate(blocks, axis=1)
    return activated, input_grad, kernel_grad
```

```python
import jax
import jax.numpy as jnp
from jax import lax
from jax.sharding import PartitionSpec as P


def passed_along(x, axis, by):
    devices = lax.axis_size(axis)
    pairs = [(i, i + by) for i in range(devices) if 0 <= i + by < devices]
    return lax.ppermute(x, axis, pairs)


def padded(block, sides, width):
    for axis, dim in sides:
        count = lax.axis_size(axis)
        forward = [(i, i + 1) for i in range(count - 1)]
        backward = [(target, source) for source, target in forward]
        low = lax.ppermute(
            lax.slice_in_dim(block, block.shape[dim] - width, None, axis=dim), axis, forward
        )
        high = lax.ppermute(lax.slice_in_dim(block, 0, width, axis=dim), axis, backward)
        block = jnp.concatenate([low, block, high], axis=dim)
    return block


def make_patches(extended):
    frames = extended.shape[0] - 2
    height = extended.shape[1] - 2
    width = extended.shape[2]
    chans = extended.shape[3]
    wide = jnp.pad(extended, ((0, 0), (0, 0), (1, 1), (0, 0)))
    patches = []
    for a in range(3):
        for b in range(3):
            parts = [wide[a : a + frames, b : b + height, c : c + width] for c in range(3)]
            patches.append(
                jnp.concatenate(parts, axis=-1).reshape(frames * height * width, 3 * chans)
            )
    return patches


def apply_taps(patches, kmat):
    total = jnp.dot(patches[0], kmat[0, 0], preferred_element_type=jnp.float32)
    for index in range(1, 9):
        total = total + jnp.dot(
            patches[index], kmat[index // 3, index % 3], preferred_element_type=jnp.float32
        )
    return total


def local(video, kernel, cotangent):
    frames, height, width, chans = video.shape
    forward_mat = kernel.reshape(3, 3, 3 * chans, chans)
    earlier = passed_along(video, "tm", 1)
    extended = padded(jnp.concatenate([earlier, video], axis=0), (("rows", 1),), 1)
    patches = make_patches(extended)
    pre = apply_taps(patches, forward_mat)
    sig = 1.0 / (1.0 + jnp.exp(-pre))
    activated = (pre * sig).astype(jnp.bfloat16).reshape(frames, height, width, chans)
    grad_flat = cotangent.reshape(frames * height * width, chans).astype(jnp.float32)
    pre_grad = (grad_flat * sig * (1.0 + pre * (1.0 - sig))).astype(jnp.bfloat16)
    pre_grid = pre_grad.reshape(frames, height, width, chans)
    later = passed_along(pre_grid, "tm", -1)
    grad_ext = padded(jnp.concatenate([pre_grid, later], axis=0), (("rows", 1),), 1)
    flipped = jnp.transpose(kernel[::-1, ::-1, ::-1], (0, 1, 2, 4, 3)).reshape(
        3, 3, 3 * chans, chans
    )
    input_grad = (
        apply_taps(make_patches(grad_ext), flipped)
        .astype(jnp.bfloat16)
        .reshape(frames, height, width, chans)
    )
    blocks = [
        lax.dot_general(
            pre_grad, piece, (((0,), (0,)), ((), ())), preferred_element_type=jnp.float32
        )
        for piece in patches
    ]
    partial_grad = jnp.concatenate(blocks, axis=1)
    owned = lax.psum_scatter(partial_grad, "tm", scatter_dimension=1, tiled=True)
    kernel_grad = lax.psum_scatter(owned, "rows", scatter_dimension=0, tiled=True)
    return (activated, input_grad, kernel_grad)


def solution(mesh):
    in_specs = (P("tm", "rows", None, None), P(), P("tm", "rows", None, None))
    out_specs = (P("tm", "rows", None, None), P("tm", "rows", None, None), P("rows", "tm"))
    return jax.shard_map(local, mesh=mesh, in_specs=in_specs, out_specs=out_specs, check_vma=False)
```

```python
import jax
import jax.numpy as jnp
from jax import lax
from jax.sharding import PartitionSpec as P


def passed_along(x, axis, by):
    devices = lax.axis_size(axis)
    pairs = [(i, i + by) for i in range(devices) if 0 <= i + by < devices]
    return lax.ppermute(x, axis, pairs)


def padded(block, sides, width):
    for axis, dim in sides:
        count = lax.axis_size(axis)
        forward = [(i, i + 1) for i in range(count - 1)]
        backward = [(target, source) for source, target in forward]
        low = lax.ppermute(
            lax.slice_in_dim(block, block.shape[dim] - width, None, axis=dim), axis, forward
        )
        high = lax.ppermute(lax.slice_in_dim(block, 0, width, axis=dim), axis, backward)
        block = jnp.concatenate([low, block, high], axis=dim)
    return block


def make_patches(extended):
    frames = extended.shape[0] - 2
    height = extended.shape[1] - 2
    width = extended.shape[2]
    chans = extended.shape[3]
    wide = jnp.pad(extended, ((0, 0), (0, 0), (1, 1), (0, 0)))
    patches = []
    for a in range(3):
        for b in range(3):
            parts = [wide[a : a + frames, b : b + height, c : c + width] for c in range(3)]
            patches.append(
                jnp.concatenate(parts, axis=-1).reshape(frames * height * width, 3 * chans)
            )
    return patches


def apply_taps(patches, kmat):
    total = jnp.dot(patches[0], kmat[0, 0], preferred_element_type=jnp.float32)
    for index in range(1, 9):
        total = total + jnp.dot(
            patches[index], kmat[index // 3, index % 3], preferred_element_type=jnp.float32
        )
    return total


def local(video, kernel, cotangent):
    frames, height, width, chans = video.shape
    forward_mat = kernel.reshape(3, 3, 3 * chans, chans)
    earlier = passed_along(video, "tm", 1)
    extended = padded(jnp.concatenate([earlier, video], axis=0), (("rows", 1),), 1)
    patches = make_patches(extended)
    pre = apply_taps(patches, forward_mat)
    sig = 1.0 / (1.0 + jnp.exp(-pre))
    activated = (pre * sig).astype(jnp.bfloat16).reshape(frames, height, width, chans)
    grad_flat = cotangent.reshape(frames * height * width, chans).astype(jnp.float32)
    pre_grad = (grad_flat * sig * (1.0 + pre * (1.0 - sig))).astype(jnp.bfloat16)
    pre_grid = pre_grad.reshape(frames, height, width, chans)
    later = passed_along(pre_grid, "tm", -1)
    grad_ext = padded(jnp.concatenate([pre_grid, later], axis=0), (("rows", 1),), 1)
    flipped = jnp.transpose(kernel[::-1, ::-1, ::-1], (0, 1, 2, 4, 3)).reshape(
        3, 3, 3 * chans, chans
    )
    input_grad = (
        apply_taps(make_patches(grad_ext), flipped)
        .astype(jnp.bfloat16)
        .reshape(frames, height, width, chans)
    )
    blocks = [
        lax.dot_general(
            pre_grad, piece, (((0,), (0,)), ((), ())), preferred_element_type=jnp.float32
        )
        for piece in patches
    ]
    partial_grad = jnp.concatenate(blocks, axis=1)
    parts = lax.axis_size("tm")
    stacked = partial_grad.reshape(partial_grad.shape[0] * parts, partial_grad.shape[1] // parts)
    kernel_grad = lax.psum_scatter(stacked, ("rows", "tm"), scatter_dimension=0, tiled=True)
    return (activated, input_grad, kernel_grad)


def solution(mesh):
    in_specs = (P("tm", "rows", None, None), P(), P("tm", "rows", None, None))
    out_specs = (P("tm", "rows", None, None), P("tm", "rows", None, None), P("rows", "tm"))
    return jax.shard_map(local, mesh=mesh, in_specs=in_specs, out_specs=out_specs, check_vma=False)
```

```python
import jax
import jax.numpy as jnp
from jax import lax
from jax.sharding import PartitionSpec as P


def passed_along(x, axis, by):
    devices = lax.axis_size(axis)
    pairs = [(i, i + by) for i in range(devices) if 0 <= i + by < devices]
    return lax.ppermute(x, axis, pairs)


def padded(block, sides, width):
    for axis, dim in sides:
        count = lax.axis_size(axis)
        forward = [(i, i + 1) for i in range(count - 1)]
        backward = [(target, source) for source, target in forward]
        low = lax.ppermute(
            lax.slice_in_dim(block, block.shape[dim] - width, None, axis=dim), axis, forward
        )
        high = lax.ppermute(lax.slice_in_dim(block, 0, width, axis=dim), axis, backward)
        block = jnp.concatenate([low, block, high], axis=dim)
    return block


def make_patches(extended):
    frames = extended.shape[0] - 2
    height = extended.shape[1] - 2
    width = extended.shape[2]
    chans = extended.shape[3]
    wide = jnp.pad(extended, ((0, 0), (0, 0), (1, 1), (0, 0)))
    patches = []
    for a in range(3):
        for b in range(3):
            parts = [wide[a : a + frames, b : b + height, c : c + width] for c in range(3)]
            patches.append(
                jnp.concatenate(parts, axis=-1).reshape(frames * height * width, 3 * chans)
            )
    return patches


def apply_taps(patches, kmat):
    total = jnp.dot(patches[0], kmat[0, 0], preferred_element_type=jnp.float32)
    for index in range(1, 9):
        total = total + jnp.dot(
            patches[index], kmat[index // 3, index % 3], preferred_element_type=jnp.float32
        )
    return total


def exchanged_half(x, axis, bit, dim):
    mine = (lax.axis_index(axis) // (1 << bit)) % 2
    pairs = [(i, i ^ (1 << bit)) for i in range(lax.axis_size(axis))]
    keep = lax.dynamic_index_in_dim(x, mine, axis=dim, keepdims=True)
    send = lax.dynamic_index_in_dim(x, 1 - mine, axis=dim, keepdims=True)
    return keep + lax.ppermute(send, axis, pairs)


def halving_scatter(partial_grad):
    outs, cols = partial_grad.shape
    tm_bits = lax.axis_size("tm").bit_length() - 1
    row_bits = lax.axis_size("rows").bit_length() - 1
    block = cols >> tm_bits
    x = partial_grad.reshape((outs,) + (2,) * tm_bits + (block,))
    for bit in range(tm_bits):
        x = exchanged_half(x, "tm", bit, tm_bits - bit)
    x = x.reshape((2,) * row_bits + (block,))
    y_bits = min(3, row_bits)
    order = []
    ys, zs = list(range(y_bits)), list(range(y_bits, row_bits))
    while ys or zs:
        if ys:
            order.append(ys.pop(0))
        if zs:
            order.append(zs.pop(0))
    for bit in order:
        x = exchanged_half(x, "rows", bit, row_bits - 1 - bit)
    return x.reshape(1, block)


def local(video, kernel, cotangent):
    frames, height, width, chans = video.shape
    forward_mat = kernel.reshape(3, 3, 3 * chans, chans)
    earlier = passed_along(video, "tm", 1)
    extended = padded(jnp.concatenate([earlier, video], axis=0), (("rows", 1),), 1)
    patches = make_patches(extended)
    pre = apply_taps(patches, forward_mat)
    sig = 1.0 / (1.0 + jnp.exp(-pre))
    activated = (pre * sig).astype(jnp.bfloat16).reshape(frames, height, width, chans)
    grad_flat = cotangent.reshape(frames * height * width, chans).astype(jnp.float32)
    pre_grad = (grad_flat * sig * (1.0 + pre * (1.0 - sig))).astype(jnp.bfloat16)
    pre_grid = pre_grad.reshape(frames, height, width, chans)
    later = passed_along(pre_grid, "tm", -1)
    grad_ext = padded(jnp.concatenate([pre_grid, later], axis=0), (("rows", 1),), 1)
    flipped = jnp.transpose(kernel[::-1, ::-1, ::-1], (0, 1, 2, 4, 3)).reshape(
        3, 3, 3 * chans, chans
    )
    input_grad = (
        apply_taps(make_patches(grad_ext), flipped)
        .astype(jnp.bfloat16)
        .reshape(frames, height, width, chans)
    )
    blocks = [
        lax.dot_general(
            pre_grad, piece, (((0,), (0,)), ((), ())), preferred_element_type=jnp.float32
        )
        for piece in patches
    ]
    partial_grad = jnp.concatenate(blocks, axis=1)
    kernel_grad = halving_scatter(partial_grad)
    return (activated, input_grad, kernel_grad)


def solution(mesh):
    in_specs = (P("tm", "rows", None, None), P(), P("tm", "rows", None, None))
    out_specs = (P("tm", "rows", None, None), P("tm", "rows", None, None), P("rows", "tm"))
    return jax.shard_map(local, mesh=mesh, in_specs=in_specs, out_specs=out_specs, check_vma=False)
```

```python
import jax
import jax.numpy as jnp
from jax import lax
from jax.sharding import PartitionSpec as P


def passed_along(x, axis, by):
    devices = lax.axis_size(axis)
    pairs = [(i, i + by) for i in range(devices) if 0 <= i + by < devices]
    return lax.ppermute(x, axis, pairs)


def padded(block, sides, width):
    for axis, dim in sides:
        count = lax.axis_size(axis)
        forward = [(i, i + 1) for i in range(count - 1)]
        backward = [(target, source) for source, target in forward]
        low = lax.ppermute(
            lax.slice_in_dim(block, block.shape[dim] - width, None, axis=dim), axis, forward
        )
        high = lax.ppermute(lax.slice_in_dim(block, 0, width, axis=dim), axis, backward)
        block = jnp.concatenate([low, block, high], axis=dim)
    return block


def make_patches(extended):
    frames = extended.shape[0] - 2
    height = extended.shape[1] - 2
    width = extended.shape[2]
    chans = extended.shape[3]
    wide = jnp.pad(extended, ((0, 0), (0, 0), (1, 1), (0, 0)))
    patches = []
    for a in range(3):
        for b in range(3):
            parts = [wide[a : a + frames, b : b + height, c : c + width] for c in range(3)]
            patches.append(
                jnp.concatenate(parts, axis=-1).reshape(frames * height * width, 3 * chans)
            )
    return patches


def apply_taps(patches, kmat):
    total = jnp.dot(patches[0], kmat[0, 0], preferred_element_type=jnp.float32)
    for index in range(1, 9):
        total = total + jnp.dot(
            patches[index], kmat[index // 3, index % 3], preferred_element_type=jnp.float32
        )
    return total


def exchanged_half(x, axis, bit, dim):
    mine = (lax.axis_index(axis) // (1 << bit)) % 2
    pairs = [(i, i ^ (1 << bit)) for i in range(lax.axis_size(axis))]
    keep = lax.dynamic_index_in_dim(x, mine, axis=dim, keepdims=True)
    send = lax.dynamic_index_in_dim(x, 1 - mine, axis=dim, keepdims=True)
    return keep + lax.ppermute(send, axis, pairs)


def halving_scatter(partial_grad):
    outs, cols = partial_grad.shape
    tm_bits = lax.axis_size("tm").bit_length() - 1
    row_bits = lax.axis_size("rows").bit_length() - 1
    block = cols >> tm_bits
    x = partial_grad.reshape((outs,) + (2,) * tm_bits + (block,))
    for bit in range(tm_bits):
        x = exchanged_half(x, "tm", bit, tm_bits - bit)
    x = x.reshape((2,) * row_bits + (block,))
    y_bits = min(3, row_bits)
    order = []
    ys, zs = list(range(y_bits)), list(range(y_bits, row_bits))
    while ys or zs:
        if ys:
            order.append(ys.pop(0))
        if zs:
            order.append(zs.pop(0))
    for bit in order:
        x = exchanged_half(x, "rows", bit, row_bits - 1 - bit)
    return x.reshape(1, block)


def exchanged_scatter(partial_grad):
    outs, cols = partial_grad.shape
    parts = lax.axis_size("tm")
    x = partial_grad.reshape(outs, parts, cols // parts)
    x = lax.all_to_all(x, "tm", 1, 1).sum(axis=1)
    x = lax.all_to_all(x, "rows", 0, 0).sum(axis=0)
    return x.reshape(1, -1)


def local(video, kernel, cotangent):
    frames, height, width, chans = video.shape
    forward_mat = kernel.reshape(3, 3, 3 * chans, chans)
    earlier = passed_along(video, "tm", 1)
    extended = padded(jnp.concatenate([earlier, video], axis=0), (("rows", 1),), 1)
    patches = make_patches(extended)
    pre = apply_taps(patches, forward_mat)
    sig = 1.0 / (1.0 + jnp.exp(-pre))
    activated = (pre * sig).astype(jnp.bfloat16).reshape(frames, height, width, chans)
    grad_flat = cotangent.reshape(frames * height * width, chans).astype(jnp.float32)
    pre_grad = (grad_flat * sig * (1.0 + pre * (1.0 - sig))).astype(jnp.bfloat16)
    pre_grid = pre_grad.reshape(frames, height, width, chans)
    later = passed_along(pre_grid, "tm", -1)
    grad_ext = padded(jnp.concatenate([pre_grid, later], axis=0), (("rows", 1),), 1)
    flipped = jnp.transpose(kernel[::-1, ::-1, ::-1], (0, 1, 2, 4, 3)).reshape(
        3, 3, 3 * chans, chans
    )
    input_grad = (
        apply_taps(make_patches(grad_ext), flipped)
        .astype(jnp.bfloat16)
        .reshape(frames, height, width, chans)
    )
    blocks = [
        lax.dot_general(
            pre_grad, piece, (((0,), (0,)), ((), ())), preferred_element_type=jnp.float32
        )
        for piece in patches
    ]
    partial_grad = jnp.concatenate(blocks, axis=1)
    kernel_grad = exchanged_scatter(partial_grad)
    return (activated, input_grad, kernel_grad)


def solution(mesh):
    in_specs = (P("tm", "rows", None, None), P(), P("tm", "rows", None, None))
    out_specs = (P("tm", "rows", None, None), P("tm", "rows", None, None), P("rows", "tm"))
    return jax.shard_map(local, mesh=mesh, in_specs=in_specs, out_specs=out_specs, check_vma=False)
```

```python
import jax
import jax.numpy as jnp
from jax import lax
from jax.sharding import Mesh, PartitionSpec as P

ROWS = ("rz", "ry")


def passed_along(x, axis, by):
    devices = lax.axis_size(axis)
    pairs = [(i, i + by) for i in range(devices) if 0 <= i + by < devices]
    return lax.ppermute(x, axis, pairs)


def padded(block, sides, width):
    for axis, dim in sides:
        count = lax.axis_size(axis)
        forward = [(i, i + 1) for i in range(count - 1)]
        backward = [(target, source) for source, target in forward]
        low = lax.ppermute(
            lax.slice_in_dim(block, block.shape[dim] - width, None, axis=dim), axis, forward
        )
        high = lax.ppermute(lax.slice_in_dim(block, 0, width, axis=dim), axis, backward)
        block = jnp.concatenate([low, block, high], axis=dim)
    return block


def make_patches(extended):
    frames = extended.shape[0] - 2
    height = extended.shape[1] - 2
    width = extended.shape[2]
    chans = extended.shape[3]
    wide = jnp.pad(extended, ((0, 0), (0, 0), (1, 1), (0, 0)))
    patches = []
    for a in range(3):
        for b in range(3):
            parts = [wide[a : a + frames, b : b + height, c : c + width] for c in range(3)]
            patches.append(
                jnp.concatenate(parts, axis=-1).reshape(frames * height * width, 3 * chans)
            )
    return patches


def apply_taps(patches, kmat):
    total = jnp.dot(patches[0], kmat[0, 0], preferred_element_type=jnp.float32)
    for index in range(1, 9):
        total = total + jnp.dot(
            patches[index], kmat[index // 3, index % 3], preferred_element_type=jnp.float32
        )
    return total


def exchanged_half(x, axis, bit, dim):
    mine = (lax.axis_index(axis) // (1 << bit)) % 2
    pairs = [(i, i ^ (1 << bit)) for i in range(lax.axis_size(axis))]
    keep = lax.dynamic_index_in_dim(x, mine, axis=dim, keepdims=True)
    send = lax.dynamic_index_in_dim(x, 1 - mine, axis=dim, keepdims=True)
    return keep + lax.ppermute(send, axis, pairs)


def halving_scatter(partial_grad):
    outs, cols = partial_grad.shape
    tm_bits = lax.axis_size("tm").bit_length() - 1
    row_bits = lax.axis_size("rows").bit_length() - 1
    block = cols >> tm_bits
    x = partial_grad.reshape((outs,) + (2,) * tm_bits + (block,))
    for bit in range(tm_bits):
        x = exchanged_half(x, "tm", bit, tm_bits - bit)
    x = x.reshape((2,) * row_bits + (block,))
    y_bits = min(3, row_bits)
    order = []
    ys, zs = list(range(y_bits)), list(range(y_bits, row_bits))
    while ys or zs:
        if ys:
            order.append(ys.pop(0))
        if zs:
            order.append(zs.pop(0))
    for bit in order:
        x = exchanged_half(x, "rows", bit, row_bits - 1 - bit)
    return x.reshape(1, block)


def exchanged_scatter(partial_grad):
    outs, cols = partial_grad.shape
    parts = lax.axis_size("tm")
    inner = lax.axis_size("ry")
    x = partial_grad.reshape(outs, parts, cols // parts)
    x = lax.all_to_all(x, "tm", 1, 1).sum(axis=1)
    x = x.reshape(outs // inner, inner, -1)
    x = lax.all_to_all(x, "ry", 1, 1).sum(axis=1)
    x = lax.all_to_all(x, "rz", 0, 0).sum(axis=0)
    return x.reshape(1, -1)


def local(video, kernel, cotangent):
    frames, height, width, chans = video.shape
    forward_mat = kernel.reshape(3, 3, 3 * chans, chans)
    earlier = passed_along(video, "tm", 1)
    extended = padded(jnp.concatenate([earlier, video], axis=0), ((ROWS, 1),), 1)
    patches = make_patches(extended)
    pre = apply_taps(patches, forward_mat)
    sig = 1.0 / (1.0 + jnp.exp(-pre))
    activated = (pre * sig).astype(jnp.bfloat16).reshape(frames, height, width, chans)
    grad_flat = cotangent.reshape(frames * height * width, chans).astype(jnp.float32)
    pre_grad = (grad_flat * sig * (1.0 + pre * (1.0 - sig))).astype(jnp.bfloat16)
    pre_grid = pre_grad.reshape(frames, height, width, chans)
    later = passed_along(pre_grid, "tm", -1)
    grad_ext = padded(jnp.concatenate([pre_grid, later], axis=0), ((ROWS, 1),), 1)
    flipped = jnp.transpose(kernel[::-1, ::-1, ::-1], (0, 1, 2, 4, 3)).reshape(
        3, 3, 3 * chans, chans
    )
    input_grad = (
        apply_taps(make_patches(grad_ext), flipped)
        .astype(jnp.bfloat16)
        .reshape(frames, height, width, chans)
    )
    blocks = [
        lax.dot_general(
            pre_grad, piece, (((0,), (0,)), ((), ())), preferred_element_type=jnp.float32
        )
        for piece in patches
    ]
    partial_grad = jnp.concatenate(blocks, axis=1)
    kernel_grad = exchanged_scatter(partial_grad)
    return (activated, input_grad, kernel_grad)


def solution(mesh):
    frames, rows = mesh.shape["tm"], mesh.shape["rows"]
    inner = 8 if rows % 8 == 0 else 1
    split = Mesh(mesh.devices.reshape(frames, rows // inner, inner), ("tm",) + ROWS)
    in_specs = (P("tm", ROWS, None, None), P(), P("tm", ROWS, None, None))
    out_specs = (P("tm", ROWS, None, None), P("tm", ROWS, None, None), P(ROWS, "tm"))
    return jax.shard_map(local, mesh=split, in_specs=in_specs, out_specs=out_specs, check_vma=False)
```

```python
import jax
import jax.numpy as jnp
from jax import lax
from jax.sharding import PartitionSpec as P


def passed_along(x, axis, by):
    devices = lax.axis_size(axis)
    pairs = [(i, i + by) for i in range(devices) if 0 <= i + by < devices]
    return lax.ppermute(x, axis, pairs)


def padded(block, sides, width):
    for axis, dim in sides:
        count = lax.axis_size(axis)
        forward = [(i, i + 1) for i in range(count - 1)]
        backward = [(target, source) for source, target in forward]
        low = lax.ppermute(
            lax.slice_in_dim(block, block.shape[dim] - width, None, axis=dim), axis, forward
        )
        high = lax.ppermute(lax.slice_in_dim(block, 0, width, axis=dim), axis, backward)
        block = jnp.concatenate([low, block, high], axis=dim)
    return block


def make_patches(extended):
    frames = extended.shape[0] - 2
    height = extended.shape[1] - 2
    width = extended.shape[2]
    chans = extended.shape[3]
    wide = jnp.pad(extended, ((0, 0), (0, 0), (1, 1), (0, 0)))
    patches = []
    for a in range(3):
        for b in range(3):
            parts = [wide[a : a + frames, b : b + height, c : c + width] for c in range(3)]
            patches.append(
                jnp.concatenate(parts, axis=-1).reshape(frames * height * width, 3 * chans)
            )
    return patches


def apply_taps(patches, kmat):
    total = jnp.dot(patches[0], kmat[0, 0], preferred_element_type=jnp.float32)
    for index in range(1, 9):
        total = total + jnp.dot(
            patches[index], kmat[index // 3, index % 3], preferred_element_type=jnp.float32
        )
    return total


def exchanged_half(x, axis, bit, dim):
    mine = (lax.axis_index(axis) // (1 << bit)) % 2
    pairs = [(i, i ^ (1 << bit)) for i in range(lax.axis_size(axis))]
    keep = lax.dynamic_index_in_dim(x, mine, axis=dim, keepdims=True)
    send = lax.dynamic_index_in_dim(x, 1 - mine, axis=dim, keepdims=True)
    return keep + lax.ppermute(send, axis, pairs)


def halving_scatter(partial_grad):
    outs, cols = partial_grad.shape
    tm_bits = lax.axis_size("tm").bit_length() - 1
    row_bits = lax.axis_size("rows").bit_length() - 1
    block = cols >> tm_bits
    x = partial_grad.reshape((outs,) + (2,) * tm_bits + (block,))
    for bit in range(tm_bits):
        x = exchanged_half(x, "tm", bit, tm_bits - bit)
    x = x.reshape((2,) * row_bits + (block,))
    y_bits = min(3, row_bits)
    order = []
    ys, zs = list(range(y_bits)), list(range(y_bits, row_bits))
    while ys or zs:
        if ys:
            order.append(ys.pop(0))
        if zs:
            order.append(zs.pop(0))
    for bit in order:
        x = exchanged_half(x, "rows", bit, row_bits - 1 - bit)
    return x.reshape(1, block)


def exchanged_scatter(partial_grad):
    outs, cols = partial_grad.shape
    parts = lax.axis_size("tm")
    x = partial_grad.reshape(outs * parts, cols // parts)
    x = lax.all_to_all(x, ("rows", "tm"), 0, 0).sum(axis=0)
    return x.reshape(1, -1)


def local(video, kernel, cotangent):
    frames, height, width, chans = video.shape
    forward_mat = kernel.reshape(3, 3, 3 * chans, chans)
    earlier = passed_along(video, "tm", 1)
    extended = padded(jnp.concatenate([earlier, video], axis=0), (("rows", 1),), 1)
    patches = make_patches(extended)
    pre = apply_taps(patches, forward_mat)
    sig = 1.0 / (1.0 + jnp.exp(-pre))
    activated = (pre * sig).astype(jnp.bfloat16).reshape(frames, height, width, chans)
    grad_flat = cotangent.reshape(frames * height * width, chans).astype(jnp.float32)
    pre_grad = (grad_flat * sig * (1.0 + pre * (1.0 - sig))).astype(jnp.bfloat16)
    pre_grid = pre_grad.reshape(frames, height, width, chans)
    later = passed_along(pre_grid, "tm", -1)
    grad_ext = padded(jnp.concatenate([pre_grid, later], axis=0), (("rows", 1),), 1)
    flipped = jnp.transpose(kernel[::-1, ::-1, ::-1], (0, 1, 2, 4, 3)).reshape(
        3, 3, 3 * chans, chans
    )
    input_grad = (
        apply_taps(make_patches(grad_ext), flipped)
        .astype(jnp.bfloat16)
        .reshape(frames, height, width, chans)
    )
    blocks = [
        lax.dot_general(
            pre_grad, piece, (((0,), (0,)), ((), ())), preferred_element_type=jnp.float32
        )
        for piece in patches
    ]
    partial_grad = jnp.concatenate(blocks, axis=1)
    kernel_grad = exchanged_scatter(partial_grad)
    return (activated, input_grad, kernel_grad)


def solution(mesh):
    in_specs = (P("tm", "rows", None, None), P(), P("tm", "rows", None, None))
    out_specs = (P("tm", "rows", None, None), P("tm", "rows", None, None), P("rows", "tm"))
    return jax.shard_map(local, mesh=mesh, in_specs=in_specs, out_specs=out_specs, check_vma=False)
```

```python
import jax
import jax.numpy as jnp
from jax import lax
from jax.sharding import PartitionSpec as P


def shifted(x, by_tm, by_rows):
    frames, rows = lax.axis_size("tm"), lax.axis_size("rows")
    pairs = [
        (m * rows + r, (m + by_tm) * rows + r + by_rows)
        for m in range(frames)
        for r in range(rows)
        if 0 <= m + by_tm < frames and 0 <= r + by_rows < rows
    ]
    return lax.ppermute(x, ("tm", "rows"), pairs)


def haloed(block, by_tm):
    last, first = block[:, -1:], block[:, :1]
    other = shifted(block, by_tm, 0)
    above = shifted(last, 0, 1)
    below = shifted(first, 0, -1)
    above_other = shifted(last, by_tm, 1)
    below_other = shifted(first, by_tm, -1)
    if by_tm > 0:
        parts = [(above_other, above), (other, block), (below_other, below)]
    else:
        parts = [(above, above_other), (block, other), (below, below_other)]
    return jnp.concatenate([jnp.concatenate(p, axis=0) for p in parts], axis=1)


def make_patches(extended):
    frames = extended.shape[0] - 2
    height = extended.shape[1] - 2
    width = extended.shape[2]
    chans = extended.shape[3]
    wide = jnp.pad(extended, ((0, 0), (0, 0), (1, 1), (0, 0)))
    patches = []
    for a in range(3):
        for b in range(3):
            parts = [wide[a : a + frames, b : b + height, c : c + width] for c in range(3)]
            patches.append(
                jnp.concatenate(parts, axis=-1).reshape(frames * height * width, 3 * chans)
            )
    return patches


def apply_taps(patches, kmat):
    total = jnp.dot(patches[0], kmat[0, 0], preferred_element_type=jnp.float32)
    for index in range(1, 9):
        total = total + jnp.dot(
            patches[index], kmat[index // 3, index % 3], preferred_element_type=jnp.float32
        )
    return total


def exchanged_scatter(partial_grad):
    outs, cols = partial_grad.shape
    parts = lax.axis_size("tm")
    x = partial_grad.reshape(outs, parts, cols // parts)
    x = lax.all_to_all(x, "tm", 1, 1).sum(axis=1)
    x = lax.all_to_all(x, "rows", 0, 0).sum(axis=0)
    return x.reshape(1, -1)


def local(video, kernel, cotangent):
    frames, height, width, chans = video.shape
    forward_mat = kernel.reshape(3, 3, 3 * chans, chans)
    extended = haloed(video, 1)
    patches = make_patches(extended)
    pre = apply_taps(patches, forward_mat)
    sig = 1.0 / (1.0 + jnp.exp(-pre))
    activated = (pre * sig).astype(jnp.bfloat16).reshape(frames, height, width, chans)
    grad_flat = cotangent.reshape(frames * height * width, chans).astype(jnp.float32)
    pre_grad = (grad_flat * sig * (1.0 + pre * (1.0 - sig))).astype(jnp.bfloat16)
    pre_grid = pre_grad.reshape(frames, height, width, chans)
    grad_ext = haloed(pre_grid, -1)
    flipped = jnp.transpose(kernel[::-1, ::-1, ::-1], (0, 1, 2, 4, 3)).reshape(
        3, 3, 3 * chans, chans
    )
    input_grad = (
        apply_taps(make_patches(grad_ext), flipped)
        .astype(jnp.bfloat16)
        .reshape(frames, height, width, chans)
    )
    blocks = [
        lax.dot_general(
            pre_grad, piece, (((0,), (0,)), ((), ())), preferred_element_type=jnp.float32
        )
        for piece in patches
    ]
    partial_grad = jnp.concatenate(blocks, axis=1)
    kernel_grad = exchanged_scatter(partial_grad)
    return (activated, input_grad, kernel_grad)


def solution(mesh):
    in_specs = (P("tm", "rows", None, None), P(), P("tm", "rows", None, None))
    out_specs = (P("tm", "rows", None, None), P("tm", "rows", None, None), P("rows", "tm"))
    return jax.shard_map(local, mesh=mesh, in_specs=in_specs, out_specs=out_specs, check_vma=False)
```

```python
import jax
import jax.numpy as jnp
from jax import lax
from jax.sharding import PartitionSpec as P


def shifted(x, by_tm, by_rows):
    frames, rows = lax.axis_size("tm"), lax.axis_size("rows")
    pairs = [
        (m * rows + r, (m + by_tm) * rows + r + by_rows)
        for m in range(frames)
        for r in range(rows)
        if 0 <= m + by_tm < frames and 0 <= r + by_rows < rows
    ]
    return lax.ppermute(x, ("tm", "rows"), pairs)


def haloed(block, by_tm):
    last, first = block[:, -1:], block[:, :1]
    other = shifted(block, by_tm, 0)
    above = shifted(last, 0, 1)
    below = shifted(first, 0, -1)
    above_other = shifted(last, by_tm, 1)
    below_other = shifted(first, by_tm, -1)
    if by_tm > 0:
        parts = [(above_other, above), (other, block), (below_other, below)]
    else:
        parts = [(above, above_other), (block, other), (below, below_other)]
    return jnp.concatenate([jnp.concatenate(p, axis=0) for p in parts], axis=1)


def make_patches(extended):
    frames = extended.shape[0] - 2
    height = extended.shape[1] - 2
    width = extended.shape[2]
    chans = extended.shape[3]
    wide = jnp.pad(extended, ((0, 0), (0, 0), (1, 1), (0, 0)))
    patches = []
    for a in range(3):
        for b in range(3):
            parts = [wide[a : a + frames, b : b + height, c : c + width] for c in range(3)]
            patches.append(
                jnp.concatenate(parts, axis=-1).reshape(frames * height * width, 3 * chans)
            )
    return patches


def apply_taps(patches, kmat):
    total = jnp.dot(patches[0], kmat[0, 0], preferred_element_type=jnp.float32)
    for index in range(1, 9):
        total = total + jnp.dot(
            patches[index], kmat[index // 3, index % 3], preferred_element_type=jnp.float32
        )
    return total


def exchanged_scatter(partial_grad):
    outs, cols = partial_grad.shape
    parts = lax.axis_size("tm")
    x = partial_grad.reshape(outs, parts, cols // parts)
    x = lax.all_to_all(x, "tm", 1, 1).sum(axis=1)
    x = lax.all_to_all(x, "rows", 0, 0).sum(axis=0)
    return x.reshape(1, -1)


def local(video, kernel, cotangent):
    frames, height, width, chans = video.shape
    both = jnp.concatenate([video, cotangent], axis=-1)
    later = shifted(both, -1, 0)
    col_video = jnp.concatenate([shifted(video, 1, 0), video, later[..., :chans]], axis=0)
    col_grad = jnp.concatenate([cotangent, later[..., chans:]], axis=0)
    flat_video = col_video.reshape(-1, width, chans)
    cut = flat_video.shape[0]

    def payload(edge):
        return jnp.concatenate([flat_video, edge.reshape(-1, width, chans)], axis=0)

    def unpacked(got):
        return got[:cut].reshape(col_video.shape), got[cut:].reshape(2 * frames, 1, width, chans)

    above_video, above_grad = unpacked(shifted(payload(col_grad[:, -1:]), 0, 1))
    below_video, below_grad = unpacked(shifted(payload(col_grad[:, :1]), 0, -1))
    footage = jnp.concatenate([above_video, col_video, below_video], axis=1)
    grad_in = jnp.concatenate([above_grad, col_grad, below_grad], axis=1)
    forward_mat = kernel.reshape(3, 3, 3 * chans, chans)
    pre = apply_taps(make_patches(footage), forward_mat)
    sig = 1.0 / (1.0 + jnp.exp(-pre))
    wide_frames, wide_rows = 2 * frames, height + 2
    grid = (wide_frames, wide_rows, width, chans)
    activated = (pre * sig).astype(jnp.bfloat16).reshape(grid)[:frames, 1 : height + 1]
    grad_flat = grad_in.reshape(-1, chans).astype(jnp.float32)
    pre_grad = (grad_flat * sig * (1.0 + pre * (1.0 - sig))).astype(jnp.bfloat16)
    grad_ext = pre_grad.reshape(grid)
    flipped = jnp.transpose(kernel[::-1, ::-1, ::-1], (0, 1, 2, 4, 3)).reshape(
        3, 3, 3 * chans, chans
    )
    input_grad = (
        apply_taps(make_patches(grad_ext), flipped)
        .astype(jnp.bfloat16)
        .reshape(frames, height, width, chans)
    )
    own_grad = grad_ext[:frames, 1 : height + 1].reshape(frames * height * width, chans)
    own_patches = make_patches(footage[: frames + 2, height - 1 : 2 * height + 1])
    blocks = [
        lax.dot_general(
            own_grad, piece, (((0,), (0,)), ((), ())), preferred_element_type=jnp.float32
        )
        for piece in own_patches
    ]
    partial_grad = jnp.concatenate(blocks, axis=1)
    kernel_grad = exchanged_scatter(partial_grad)
    return (activated, input_grad, kernel_grad)


def solution(mesh):
    in_specs = (P("tm", "rows", None, None), P(), P("tm", "rows", None, None))
    out_specs = (P("tm", "rows", None, None), P("tm", "rows", None, None), P("rows", "tm"))
    return jax.shard_map(local, mesh=mesh, in_specs=in_specs, out_specs=out_specs, check_vma=False)
```

```python
import jax
import jax.numpy as jnp
from jax import lax
from jax.sharding import PartitionSpec as P


def passed_along(x, axis, by):
    devices = lax.axis_size(axis)
    pairs = [(i, i + by) for i in range(devices) if 0 <= i + by < devices]
    return lax.ppermute(x, axis, pairs)


def padded(block, sides, width):
    for axis, dim in sides:
        count = lax.axis_size(axis)
        forward = [(i, i + 1) for i in range(count - 1)]
        backward = [(target, source) for source, target in forward]
        low = lax.ppermute(
            lax.slice_in_dim(block, block.shape[dim] - width, None, axis=dim), axis, forward
        )
        high = lax.ppermute(lax.slice_in_dim(block, 0, width, axis=dim), axis, backward)
        block = jnp.concatenate([low, block, high], axis=dim)
    return block


def make_patches(extended):
    frames = extended.shape[0] - 2
    height = extended.shape[1] - 2
    width = extended.shape[2]
    chans = extended.shape[3]
    wide = jnp.pad(extended, ((0, 0), (0, 0), (1, 1), (0, 0)))
    patches = []
    for a in range(3):
        for b in range(3):
            parts = [wide[a : a + frames, b : b + height, c : c + width] for c in range(3)]
            patches.append(
                jnp.concatenate(parts, axis=-1).reshape(frames * height * width, 3 * chans)
            )
    return patches


def apply_taps(patches, kmat):
    total = jnp.dot(patches[0], kmat[0, 0], preferred_element_type=jnp.float32)
    for index in range(1, 9):
        total = total + jnp.dot(
            patches[index], kmat[index // 3, index % 3], preferred_element_type=jnp.float32
        )
    return total


def tm_summed(partial_grad):
    outs, cols = partial_grad.shape
    parts = lax.axis_size("tm")
    x = partial_grad.reshape(outs, parts, cols // parts)
    return lax.all_to_all(x, "tm", 1, 1).sum(axis=1)


def local(video, kernel, cotangent):
    frames, height, width, chans = video.shape
    forward_mat = kernel.reshape(3, 3, 3 * chans, chans)
    earlier = passed_along(video, "tm", 1)
    extended = padded(jnp.concatenate([earlier, video], axis=0), (("rows", 1),), 1)
    patches = make_patches(extended)
    pre = apply_taps(patches, forward_mat)
    sig = 1.0 / (1.0 + jnp.exp(-pre))
    activated = (pre * sig).astype(jnp.bfloat16).reshape(frames, height, width, chans)
    grad_flat = cotangent.reshape(frames * height * width, chans).astype(jnp.float32)
    pre_grad = (grad_flat * sig * (1.0 + pre * (1.0 - sig))).astype(jnp.bfloat16)
    blocks = [
        lax.dot_general(
            pre_grad, piece, (((0,), (0,)), ((), ())), preferred_element_type=jnp.float32
        )
        for piece in patches
    ]
    summed = tm_summed(jnp.concatenate(blocks, axis=1))
    summed, pre_grad = lax.optimization_barrier((summed, pre_grad))
    kernel_grad = lax.all_to_all(summed, "rows", 0, 0).sum(axis=0).reshape(1, -1)
    pre_grid = pre_grad.reshape(frames, height, width, chans)
    later = passed_along(pre_grid, "tm", -1)
    grad_ext = padded(jnp.concatenate([pre_grid, later], axis=0), (("rows", 1),), 1)
    flipped = jnp.transpose(kernel[::-1, ::-1, ::-1], (0, 1, 2, 4, 3)).reshape(
        3, 3, 3 * chans, chans
    )
    input_grad = (
        apply_taps(make_patches(grad_ext), flipped)
        .astype(jnp.bfloat16)
        .reshape(frames, height, width, chans)
    )
    return (activated, input_grad, kernel_grad)


def solution(mesh):
    in_specs = (P("tm", "rows", None, None), P(), P("tm", "rows", None, None))
    out_specs = (P("tm", "rows", None, None), P("tm", "rows", None, None), P("rows", "tm"))
    return jax.shard_map(local, mesh=mesh, in_specs=in_specs, out_specs=out_specs, check_vma=False)
```

```python
import jax
import jax.numpy as jnp
from jax import lax
from jax.sharding import PartitionSpec as P


def passed_along(x, axis, by):
    devices = lax.axis_size(axis)
    pairs = [(i, i + by) for i in range(devices) if 0 <= i + by < devices]
    return lax.ppermute(x, axis, pairs)


def padded(block, sides, width):
    for axis, dim in sides:
        count = lax.axis_size(axis)
        forward = [(i, i + 1) for i in range(count - 1)]
        backward = [(target, source) for source, target in forward]
        low = lax.ppermute(
            lax.slice_in_dim(block, block.shape[dim] - width, None, axis=dim), axis, forward
        )
        high = lax.ppermute(lax.slice_in_dim(block, 0, width, axis=dim), axis, backward)
        block = jnp.concatenate([low, block, high], axis=dim)
    return block


def make_patches(extended):
    frames = extended.shape[0] - 2
    height = extended.shape[1] - 2
    width = extended.shape[2]
    chans = extended.shape[3]
    wide = jnp.pad(extended, ((0, 0), (0, 0), (1, 1), (0, 0)))
    patches = []
    for a in range(3):
        for b in range(3):
            parts = [wide[a : a + frames, b : b + height, c : c + width] for c in range(3)]
            patches.append(
                jnp.concatenate(parts, axis=-1).reshape(frames * height * width, 3 * chans)
            )
    return patches


def apply_taps(patches, kmat):
    total = jnp.dot(patches[0], kmat[0, 0], preferred_element_type=jnp.float32)
    for index in range(1, 9):
        total = total + jnp.dot(
            patches[index], kmat[index // 3, index % 3], preferred_element_type=jnp.float32
        )
    return total


def exchanged_scatter(partial_grad):
    outs, cols = partial_grad.shape
    parts = lax.axis_size("tm")
    x = partial_grad.reshape(outs, parts, cols // parts)
    x = lax.all_to_all(x, "tm", 1, 1).sum(axis=1)
    x = lax.all_to_all(x, "rows", 0, 0).sum(axis=0)
    return x.reshape(1, -1)


def local(video, kernel, cotangent):
    frames, height, width, chans = video.shape
    forward_mat = kernel.reshape(3, 3, 3 * chans, chans)
    earlier = passed_along(video, "tm", 1)
    later = passed_along(jnp.concatenate([video, cotangent], axis=-1), "tm", -1)
    column = jnp.concatenate([earlier, video, later[..., :chans]], axis=0)
    extended = padded(column, (("rows", 1),), 1)
    patches = make_patches(extended)
    pre = apply_taps(patches, forward_mat)
    sig = 1.0 / (1.0 + jnp.exp(-pre))
    own = frames * height * width
    activated = (pre[:own] * sig[:own]).astype(jnp.bfloat16).reshape(frames, height, width, chans)
    grad_in = jnp.concatenate([cotangent, later[..., chans:]], axis=0)
    grad_flat = grad_in.reshape(-1, chans).astype(jnp.float32)
    pre_grad = (grad_flat * sig * (1.0 + pre * (1.0 - sig))).astype(jnp.bfloat16)
    pre_grid = pre_grad.reshape(2 * frames, height, width, chans)
    grad_ext = padded(pre_grid, (("rows", 1),), 1)
    flipped = jnp.transpose(kernel[::-1, ::-1, ::-1], (0, 1, 2, 4, 3)).reshape(
        3, 3, 3 * chans, chans
    )
    input_grad = (
        apply_taps(make_patches(grad_ext), flipped)
        .astype(jnp.bfloat16)
        .reshape(frames, height, width, chans)
    )
    blocks = [
        lax.dot_general(
            pre_grad[:own], piece[:own], (((0,), (0,)), ((), ())), preferred_element_type=jnp.float32
        )
        for piece in patches
    ]
    partial_grad = jnp.concatenate(blocks, axis=1)
    kernel_grad = exchanged_scatter(partial_grad)
    return (activated, input_grad, kernel_grad)


def solution(mesh):
    in_specs = (P("tm", "rows", None, None), P(), P("tm", "rows", None, None))
    out_specs = (P("tm", "rows", None, None), P("tm", "rows", None, None), P("rows", "tm"))
    return jax.shard_map(local, mesh=mesh, in_specs=in_specs, out_specs=out_specs, check_vma=False)
```

```python
import jax
import jax.numpy as jnp
from jax import lax
from jax.sharding import PartitionSpec as P


def passed_along(x, axis, by):
    devices = lax.axis_size(axis)
    pairs = [(i, i + by) for i in range(devices) if 0 <= i + by < devices]
    return lax.ppermute(x, axis, pairs)


def padded(block, sides, width):
    for axis, dim in sides:
        count = lax.axis_size(axis)
        forward = [(i, i + 1) for i in range(count - 1)]
        backward = [(target, source) for source, target in forward]
        low = lax.ppermute(
            lax.slice_in_dim(block, block.shape[dim] - width, None, axis=dim), axis, forward
        )
        high = lax.ppermute(lax.slice_in_dim(block, 0, width, axis=dim), axis, backward)
        block = jnp.concatenate([low, block, high], axis=dim)
    return block


def make_patches(extended):
    frames = extended.shape[0] - 2
    height = extended.shape[1] - 2
    width = extended.shape[2]
    chans = extended.shape[3]
    wide = jnp.pad(extended, ((0, 0), (0, 0), (1, 1), (0, 0)))
    patches = []
    for a in range(3):
        for b in range(3):
            parts = [wide[a : a + frames, b : b + height, c : c + width] for c in range(3)]
            patches.append(
                jnp.concatenate(parts, axis=-1).reshape(frames * height * width, 3 * chans)
            )
    return patches


def apply_taps(patches, kmat):
    total = jnp.dot(patches[0], kmat[0, 0], preferred_element_type=jnp.float32)
    for index in range(1, 9):
        total = total + jnp.dot(
            patches[index], kmat[index // 3, index % 3], preferred_element_type=jnp.float32
        )
    return total


def exchanged_scatter(partial_t):
    cols, outs = partial_t.shape
    parts = lax.axis_size("tm")
    x = partial_t.reshape(parts, cols // parts, outs)
    x = lax.all_to_all(x, "tm", 0, 0).sum(axis=0)
    x = lax.all_to_all(x.T, "rows", 0, 0).sum(axis=0)
    return x.reshape(1, -1)


def local(video, kernel, cotangent):
    frames, height, width, chans = video.shape
    forward_mat = kernel.reshape(3, 3, 3 * chans, chans)
    earlier = passed_along(video, "tm", 1)
    extended = padded(jnp.concatenate([earlier, video], axis=0), (("rows", 1),), 1)
    patches = make_patches(extended)
    pre = apply_taps(patches, forward_mat)
    sig = 1.0 / (1.0 + jnp.exp(-pre))
    activated = (pre * sig).astype(jnp.bfloat16).reshape(frames, height, width, chans)
    grad_flat = cotangent.reshape(frames * height * width, chans).astype(jnp.float32)
    pre_grad = (grad_flat * sig * (1.0 + pre * (1.0 - sig))).astype(jnp.bfloat16)
    pre_grid = pre_grad.reshape(frames, height, width, chans)
    later = passed_along(pre_grid, "tm", -1)
    grad_ext = padded(jnp.concatenate([pre_grid, later], axis=0), (("rows", 1),), 1)
    flipped = jnp.transpose(kernel[::-1, ::-1, ::-1], (0, 1, 2, 4, 3)).reshape(
        3, 3, 3 * chans, chans
    )
    input_grad = (
        apply_taps(make_patches(grad_ext), flipped)
        .astype(jnp.bfloat16)
        .reshape(frames, height, width, chans)
    )
    blocks = [
        lax.dot_general(
            piece, pre_grad, (((0,), (0,)), ((), ())), preferred_element_type=jnp.float32
        )
        for piece in patches
    ]
    partial_grad = jnp.concatenate(blocks, axis=0)
    kernel_grad = exchanged_scatter(partial_grad)
    return (activated, input_grad, kernel_grad)


def solution(mesh):
    in_specs = (P("tm", "rows", None, None), P(), P("tm", "rows", None, None))
    out_specs = (P("tm", "rows", None, None), P("tm", "rows", None, None), P("rows", "tm"))
    return jax.shard_map(local, mesh=mesh, in_specs=in_specs, out_specs=out_specs, check_vma=False)
```

```python
import jax
import jax.numpy as jnp
from jax import lax
from jax.sharding import PartitionSpec as P


def passed_along(x, axis, by):
    devices = lax.axis_size(axis)
    pairs = [(i, i + by) for i in range(devices) if 0 <= i + by < devices]
    return lax.ppermute(x, axis, pairs)


def padded(block, sides, width):
    for axis, dim in sides:
        count = lax.axis_size(axis)
        forward = [(i, i + 1) for i in range(count - 1)]
        backward = [(target, source) for source, target in forward]
        low = lax.ppermute(
            lax.slice_in_dim(block, block.shape[dim] - width, None, axis=dim), axis, forward
        )
        high = lax.ppermute(lax.slice_in_dim(block, 0, width, axis=dim), axis, backward)
        block = jnp.concatenate([low, block, high], axis=dim)
    return block


def make_patches(extended):
    frames = extended.shape[0] - 2
    height = extended.shape[1] - 2
    width = extended.shape[2]
    chans = extended.shape[3]
    wide = jnp.pad(extended, ((0, 0), (0, 0), (1, 1), (0, 0)))
    patches = []
    for a in range(3):
        for b in range(3):
            parts = [wide[a : a + frames, b : b + height, c : c + width] for c in range(3)]
            patches.append(
                jnp.concatenate(parts, axis=-1).reshape(frames * height * width, 3 * chans)
            )
    return patches


def apply_taps(patches, kmat):
    total = jnp.dot(patches[0], kmat[0, 0], preferred_element_type=jnp.float32)
    for index in range(1, 9):
        total = total + jnp.dot(
            patches[index], kmat[index // 3, index % 3], preferred_element_type=jnp.float32
        )
    return total


def exchanged_scatter(partial_grad):
    outs, cols = partial_grad.shape
    parts = lax.axis_size("tm")
    x = lax.all_to_all(partial_grad, "rows", 0, 0).sum(axis=0)
    x = lax.all_to_all(x.reshape(parts, cols // parts), "tm", 0, 0).sum(axis=0)
    return x.reshape(1, -1)


def local(video, kernel, cotangent):
    frames, height, width, chans = video.shape
    forward_mat = kernel.reshape(3, 3, 3 * chans, chans)
    earlier = passed_along(video, "tm", 1)
    extended = padded(jnp.concatenate([earlier, video], axis=0), (("rows", 1),), 1)
    patches = make_patches(extended)
    pre = apply_taps(patches, forward_mat)
    sig = 1.0 / (1.0 + jnp.exp(-pre))
    activated = (pre * sig).astype(jnp.bfloat16).reshape(frames, height, width, chans)
    grad_flat = cotangent.reshape(frames * height * width, chans).astype(jnp.float32)
    pre_grad = (grad_flat * sig * (1.0 + pre * (1.0 - sig))).astype(jnp.bfloat16)
    pre_grid = pre_grad.reshape(frames, height, width, chans)
    later = passed_along(pre_grid, "tm", -1)
    grad_ext = padded(jnp.concatenate([pre_grid, later], axis=0), (("rows", 1),), 1)
    flipped = jnp.transpose(kernel[::-1, ::-1, ::-1], (0, 1, 2, 4, 3)).reshape(
        3, 3, 3 * chans, chans
    )
    input_grad = (
        apply_taps(make_patches(grad_ext), flipped)
        .astype(jnp.bfloat16)
        .reshape(frames, height, width, chans)
    )
    blocks = [
        lax.dot_general(
            pre_grad, piece, (((0,), (0,)), ((), ())), preferred_element_type=jnp.float32
        )
        for piece in patches
    ]
    partial_grad = jnp.concatenate(blocks, axis=1)
    kernel_grad = exchanged_scatter(partial_grad)
    return (activated, input_grad, kernel_grad)


def solution(mesh):
    in_specs = (P("tm", "rows", None, None), P(), P("tm", "rows", None, None))
    out_specs = (P("tm", "rows", None, None), P("tm", "rows", None, None), P("rows", "tm"))
    return jax.shard_map(local, mesh=mesh, in_specs=in_specs, out_specs=out_specs, check_vma=False)
```

```python
import jax
import jax.numpy as jnp
from jax import lax
from jax.sharding import PartitionSpec as P


def passed_along(x, axis, by):
    devices = lax.axis_size(axis)
    pairs = [(i, i + by) for i in range(devices) if 0 <= i + by < devices]
    return lax.ppermute(x, axis, pairs)


def padded(block, sides, width):
    for axis, dim in sides:
        count = lax.axis_size(axis)
        forward = [(i, i + 1) for i in range(count - 1)]
        backward = [(target, source) for source, target in forward]
        low = lax.ppermute(
            lax.slice_in_dim(block, block.shape[dim] - width, None, axis=dim), axis, forward
        )
        high = lax.ppermute(lax.slice_in_dim(block, 0, width, axis=dim), axis, backward)
        block = jnp.concatenate([low, block, high], axis=dim)
    return block


def make_patches(extended):
    frames = extended.shape[0] - 2
    height = extended.shape[1] - 2
    width = extended.shape[2]
    chans = extended.shape[3]
    wide = jnp.pad(extended, ((0, 0), (0, 0), (1, 1), (0, 0)))
    patches = []
    for a in range(3):
        for b in range(3):
            parts = [wide[a : a + frames, b : b + height, c : c + width] for c in range(3)]
            patches.append(
                jnp.concatenate(parts, axis=-1).reshape(frames * height * width, 3 * chans)
            )
    return patches


def apply_taps(patches, kmat):
    total = jnp.dot(patches[0], kmat[0, 0], preferred_element_type=jnp.float32)
    for index in range(1, 9):
        total = total + jnp.dot(
            patches[index], kmat[index // 3, index % 3], preferred_element_type=jnp.float32
        )
    return total


def exchanged_scatter(partial_t):
    cols, outs = partial_t.shape
    parts = lax.axis_size("tm")
    x = partial_t.reshape(parts, cols // parts, outs)
    x = lax.all_to_all(x, "tm", 0, 0).sum(axis=0)
    x = lax.all_to_all(x.T, "rows", 0, 0).sum(axis=0)
    return x.reshape(1, -1)


def local(video, kernel, cotangent):
    frames, height, width, chans = video.shape
    forward_mat = kernel.reshape(3, 3, 3 * chans, chans)
    earlier = passed_along(video, "tm", 1)
    later = passed_along(jnp.concatenate([video, cotangent], axis=-1), "tm", -1)
    column = jnp.concatenate([earlier, video, later[..., :chans]], axis=0)
    extended = padded(column, (("rows", 1),), 1)
    patches = make_patches(extended)
    pre = apply_taps(patches, forward_mat)
    sig = 1.0 / (1.0 + jnp.exp(-pre))
    own = frames * height * width
    activated = (pre[:own] * sig[:own]).astype(jnp.bfloat16).reshape(frames, height, width, chans)
    grad_in = jnp.concatenate([cotangent, later[..., chans:]], axis=0)
    grad_flat = grad_in.reshape(-1, chans).astype(jnp.float32)
    pre_grad = (grad_flat * sig * (1.0 + pre * (1.0 - sig))).astype(jnp.bfloat16)
    pre_grid = pre_grad.reshape(2 * frames, height, width, chans)
    grad_ext = padded(pre_grid, (("rows", 1),), 1)
    flipped = jnp.transpose(kernel[::-1, ::-1, ::-1], (0, 1, 2, 4, 3)).reshape(
        3, 3, 3 * chans, chans
    )
    input_grad = (
        apply_taps(make_patches(grad_ext), flipped)
        .astype(jnp.bfloat16)
        .reshape(frames, height, width, chans)
    )
    blocks = [
        lax.dot_general(
            piece[:own], pre_grad[:own], (((0,), (0,)), ((), ())), preferred_element_type=jnp.float32
        )
        for piece in patches
    ]
    partial_grad = jnp.concatenate(blocks, axis=0)
    kernel_grad = exchanged_scatter(partial_grad)
    return (activated, input_grad, kernel_grad)


def solution(mesh):
    in_specs = (P("tm", "rows", None, None), P(), P("tm", "rows", None, None))
    out_specs = (P("tm", "rows", None, None), P("tm", "rows", None, None), P("rows", "tm"))
    return jax.shard_map(local, mesh=mesh, in_specs=in_specs, out_specs=out_specs, check_vma=False)
```
